128 devices in a mesh: gx: 4 (over z), gy: 32 (over y, x, core).
Axes of the slice: x: 4, y: 4, z: 4, core: 2. Of those that a mesh axis runs over, the one named last changes fastest.
Arguments:
- tokens: bfloat16 [32768, 1664], P('gy', 'gx'), may hold values from -6 to 6
- segment_ids: int32 [32768], P('gy'), may hold values from 0 to 1023, as said below
- first_gain: float32 [1664], replicated, may hold values from 0.5 to 2
- first_bias: float32 [1664], replicated, may hold values from -3 to 3
- query_key_value: bfloat16 [3, 1664, 1664], P(None, 'gy', 'gx'), may hold values from -0.15625 to 0.15625
- project_out: bfloat16 [1664, 1664], P('gx', 'gy'), may hold values from -0.15625 to 0.15625
- second_gain: float32 [1664], replicated, may hold values from 0.5 to 2
- second_bias: float32 [1664], replicated, may hold values from -3 to 3
- up_weight: bfloat16 [1664, 8192], P('gy', 'gx'), may hold values from -0.15625 to 0.15625
- down_weight: bfloat16 [8192, 1664], P('gx', 'gy'), may hold values from -0.0625 to 0.0625
- final_gain: float32 [1664], replicated, may hold values from 0.5 to 2
- final_bias: float32 [1664], replicated, may hold values from -3 to 3
- merge_weight: bfloat16 [4, 1664, 1664], P(None, 'gx', 'gy'), may hold values from -0.078125 to 0.078125
- owners: int32 [8192, 1], P('gy'), may hold values from 0 to 31; in each aligned block of 256 rows (0 to 255, 256 to 511, ...) at most 16 rows name the same one
Outputs:
- delivered: bfloat16 [32, 32, 16, 1664], P('gy', None, None, 'gx')
The draws below stay inside these ranges and needn't reach their ends.
Inputs may be any that keep to these rules, and one draw needn't show every extreme that they name: `segment_ids`: each segment is a run of whole units of 32 consecutive tokens that lies inside one aligned block of 1024 tokens; ids never fall along the tokens and differ between segments. `owners`: in each aligned block of 256 rows (the merged tokens of one index of gy), no owner is named by more than 16 rows.
All inputs are finite; a program needn't handle non-finite values.
Results may differ from the reference program's by a relative error of at most 0.02.
Values may be sent and summed in bfloat16 or wider, within the bound.
No kernel may reach another device: no remote copies, remote signals or barrier semaphores. Data moves between devices by JAX's collectives and lax.ppermute only.
A program may use at most 128 MiB of HBM per device.

```python
import math
import jax
import jax.numpy as jnp
import numpy as np
from jax import lax

D = 1664
HEADS = 16
HEAD = 104
FF = 8192
IMG_W = 16
TOK_DEV = 1024
TOKENS = 32768
MERGED_DEV = 256
MERGED = 8192
CAP = 16
N_GY = 32


def draw_segment_ids(key, part):
    unit_count = TOKENS // (2 * IMG_W)
    per_block = TOK_DEV // (2 * IMG_W)
    coin = jax.random.randint(key, (unit_count,), 0, 3)
    unit_index = jnp.arange(unit_count, dtype=jnp.int32)
    forced = (unit_index % per_block == 0) | (unit_index == unit_count - 1)
    starts = forced | (coin == 0)
    first_unit = lax.cummax(jnp.where(starts, unit_index, 0).astype(jnp.int32), axis=0)
    return jnp.repeat(first_unit, 2 * IMG_W).astype(jnp.int32)


def level_of(own_key, extent, cuts, least, largest):
    level, own = 1.0, jax.random.fold_in(own_key, 6)
    for position, parts in cuts:
        heights = jnp.exp(jax.random.uniform(jax.random.fold_in(own, position), (parts,), jnp.float32, least / len(cuts), largest / len(cuts)))
        level = level * jnp.repeat(heights, extent[position] // parts).reshape([-1 if axis == position else 1 for axis in range(len(extent))])
    return level


def deal_out(key, own, number, rows, number_of, top, limit, slope):
    ranking = jax.random.permutation(key, number_of)
    heavy_load, ordinary = portions_of(number_of, rows * top, limit, slope, True), portions_of(number_of, rows * top, limit, slope, False)
    places = jnp.arange(number_of)

    def named(sizes, turn):
        used = int((sizes > 0).sum())
        fixed = max(1, used // 4)
        passed = fixed + (places - fixed + turn * (used - fixed)) % max(1, number_of - fixed)
        return jnp.zeros((number_of,), jnp.int32).at[ranking[jnp.where(places < fixed, places, passed)]].set(jnp.asarray(sizes, jnp.int32))

    sizes = jnp.where(number % 4 == 0, named(heavy_load, number // 4), named(ordinary, number - number // 4 - 1))
    mixed = jax.random.permutation(jax.random.fold_in(own, 3), number_of)
    source_of, sink = mixed[0:number_of // 2 * 2:2], mixed[1:number_of // 2 * 2:2]
    slack = jnp.minimum(sizes[source_of] - 1, limit - sizes[sink]) // 2
    slack = jnp.where((source_of == ranking[0]) | (sink == ranking[0]) | (sizes[sink] == 0), 0, jnp.maximum(slack, 0))
    passed = jax.random.randint(jax.random.fold_in(own, 4), (number_of // 2,), 0, 1 << 20) % (slack + 1)
    sizes = sizes.at[source_of].add(-passed).at[sink].add(passed)
    items = jnp.searchsorted(jnp.cumsum(sizes), jnp.arange(rows * top), side="right").astype(jnp.int32)
    table = items.reshape(top, rows).T
    table = table[jax.random.permutation(jax.random.fold_in(own, 1), rows)]
    turn = jax.random.randint(jax.random.fold_in(own, 2), (rows, 1), 0, top)
    return jnp.take_along_axis(table, (jnp.arange(top)[None, :] + turn) % top, axis=1)


def portions_of(amount, total, bound, lean, full):
    loads = [(1 << 20) // math.isqrt(grade ** lean) + 1 for grade in range(1, amount + 1)]
    largest = bound if full else min(bound, max(-(-total // amount), total * loads[0] // sum(loads)))
    least = 1 if total - largest >= amount - 1 else 0
    given, spare = [largest] + [least] * (amount - 1), total - largest - least * (amount - 1)
    while spare > 0:
        movable = [i for i in range(1, amount) if given[i] < largest] or [i for i in range(1, amount) if given[i] < bound]
        whole, remaining = sum([loads[i] for i in movable]), spare
        for i in movable:
            extra = min(bound - given[i], max(1, remaining * loads[i] // whole), spare)
            given[i] = given[i] + extra
            spare = spare - extra
    return np.array(given)


def scatter_about(rng, dims, scale, bound, split=(), held_as=jnp.bfloat16):
    values = scale * jax.random.normal(rng, dims, jnp.float32)
    if split:
        values = values * level_of(rng, dims, split, -0.22, 0.18)
    return jnp.clip(values, -bound, bound).astype(held_as)


def setup_inputs(seed: int = 0) -> dict:
    splits = jax.random.split(jax.random.key(seed), 15)
    tokens = scatter_about(splits[0], (TOKENS, D), 1.0, 6.0, ((0, 32), (1, 4)))
    segment_ids = draw_segment_ids(jax.random.fold_in(splits[14], 71), 0)
    first_gain = jnp.clip(jnp.exp(jax.random.uniform(splits[2], (D,), jnp.float32, math.log(0.5), math.log(2.0))), 0.5, 2.0)
    first_bias = scatter_about(splits[3], (D,), 0.5, 3.0, (), jnp.float32)
    query_key_value = scatter_about(splits[4], (3, D, D), D ** -0.5, 0.15625, ((1, 32), (2, 4)))
    project_out = scatter_about(splits[5], (D, D), D ** -0.5, 0.15625, ((0, 4), (1, 32)))
    second_gain = jnp.clip(jnp.exp(jax.random.uniform(splits[6], (D,), jnp.float32, math.log(0.5), math.log(2.0))), 0.5, 2.0)
    second_bias = scatter_about(splits[7], (D,), 0.5, 3.0, (), jnp.float32)
    up_weight = scatter_about(splits[8], (D, FF), D ** -0.5, 0.15625, ((0, 32), (1, 4)))
    down_weight = scatter_about(splits[9], (FF, D), FF ** -0.5, 0.0625, ((0, 4), (1, 32)))
    final_gain = jnp.clip(jnp.exp(jax.random.uniform(splits[10], (D,), jnp.float32, math.log(0.5), math.log(2.0))), 0.5, 2.0)
    final_bias = scatter_about(splits[11], (D,), 0.5, 3.0, (), jnp.float32)
    merge_weight = scatter_about(splits[12], (4, D, D), (4 * D) ** -0.5, 0.078125, ((1, 4), (2, 32)))
    owners_keys = jax.random.split(jax.random.fold_in(splits[13], 1), MERGED // MERGED_DEV)
    owners_turns = jax.random.permutation(jax.random.fold_in(splits[13], 3), MERGED // MERGED_DEV)
    owners = jax.vmap(lambda own, number: deal_out(jax.random.fold_in(splits[13], 2), own, number, MERGED_DEV, N_GY, 1, CAP, 2))(owners_keys, owners_turns).reshape((MERGED, 1))
    return {"tokens": tokens, "segment_ids": segment_ids, "first_gain": first_gain, "first_bias": first_bias, "query_key_value": query_key_value, "project_out": project_out, "second_gain": second_gain, "second_bias": second_bias, "up_weight": up_weight, "down_weight": down_weight, "final_gain": final_gain, "final_bias": final_bias, "merge_weight": merge_weight, "owners": owners}


EPSILON = 1e-06

def layer_norm(values, gain, bias):
    values = values.astype(jnp.float32)
    center = values - lax.optimization_barrier(jnp.mean(values, axis=-1, keepdims=True))
    spread = lax.optimization_barrier(jnp.mean(center * center, axis=-1, keepdims=True))
    return center * lax.rsqrt(spread + EPSILON) * gain + bias

def attend(query_rows, key_rows, value_rows, query_ids, key_ids):
    scores = jnp.einsum('qhe,khe->hqk', query_rows.astype(jnp.float32), key_rows.astype(jnp.float32)) * HEAD ** (-0.5)
    same_segment = query_ids[None, :, None] == key_ids[None, None, :]
    scores = jnp.where(same_segment, scores, -1e+30)
    highest = lax.optimization_barrier(jnp.max(scores, axis=-1, keepdims=True))
    raised = jnp.exp(scores - highest)
    shares = (raised / lax.optimization_barrier(jnp.sum(raised, axis=-1, keepdims=True))).astype(jnp.bfloat16)
    return jnp.einsum('hqk,khe->qhe', shares.astype(jnp.float32), value_rows.astype(jnp.float32)).astype(jnp.bfloat16)

def reference(tokens, segment_ids, first_gain, first_bias, query_key_value, project_out, second_gain, second_bias, up_weight, down_weight, final_gain, final_bias, merge_weight, owners):
    normed = layer_norm(tokens, first_gain, first_bias).astype(jnp.bfloat16)
    qkv = jnp.einsum('td,kdc->ktc', normed.astype(jnp.float32), query_key_value.astype(jnp.float32)).astype(jnp.bfloat16)
    queries = qkv[0].reshape(TOKENS, HEADS, HEAD)
    key_all = qkv[1].reshape(TOKENS, HEADS, HEAD)
    value_all = qkv[2].reshape(TOKENS, HEADS, HEAD)
    query_block = min(512, TOK_DEV)

    def one_block(index):
        first_query = index * query_block
        first_key = first_query // TOK_DEV * TOK_DEV
        query_rows = lax.dynamic_slice_in_dim(queries, first_query, query_block, 0)
        key_rows = lax.dynamic_slice_in_dim(key_all, first_key, TOK_DEV, 0)
        value_rows = lax.dynamic_slice_in_dim(value_all, first_key, TOK_DEV, 0)
        query_ids = lax.dynamic_slice_in_dim(segment_ids, first_query, query_block, 0)
        key_ids = lax.dynamic_slice_in_dim(segment_ids, first_key, TOK_DEV, 0)
        return attend(query_rows, key_rows, value_rows, query_ids, key_ids)
    attended = lax.map(one_block, jnp.arange(TOKENS // query_block, dtype=jnp.int32)).reshape(TOKENS, D)
    first_resid = (tokens.astype(jnp.float32) + jnp.dot(attended, project_out, preferred_element_type=jnp.float32)).astype(jnp.bfloat16)
    second_normed = layer_norm(first_resid, second_gain, second_bias).astype(jnp.bfloat16)
    upper = jnp.dot(second_normed, up_weight, preferred_element_type=jnp.float32)
    hidden = jax.nn.gelu(upper, approximate=False).astype(jnp.bfloat16)
    second_resid = (first_resid.astype(jnp.float32) + jnp.dot(hidden, down_weight, preferred_element_type=jnp.float32)).astype(jnp.bfloat16)
    final_normed = layer_norm(second_resid, final_gain, final_bias).astype(jnp.bfloat16)
    grouped = final_normed.reshape(TOKENS // (2 * IMG_W), 2, IMG_W // 2, 2, D).transpose(0, 2, 1, 3, 4).reshape(MERGED, 4, D)
    projected = jnp.einsum('pkf,kfc->pc', grouped.astype(jnp.float32), merge_weight.astype(jnp.float32)).astype(jnp.bfloat16)
    owner_col = owners[:, 0].astype(jnp.int32)
    one_hot = (owner_col[:, None] == jnp.arange(N_GY, dtype=jnp.int32)[None, :]).astype(jnp.int32)
    one_hot = one_hot.reshape(N_GY, MERGED_DEV, N_GY)
    slot_rank = lax.optimization_barrier(jnp.sum((jnp.cumsum(one_hot, axis=1) - 1) * one_hot, axis=-1)).reshape(MERGED).astype(jnp.int32)
    source_idx = (jnp.arange(MERGED, dtype=jnp.int32) // MERGED_DEV).astype(jnp.int32)
    delivered = jnp.zeros((N_GY, N_GY, CAP, D), jnp.bfloat16).at[owner_col, source_idx, slot_rank].set(projected)
    return delivered
```

```python
import jax
import jax.numpy as jnp
from jax import lax
from jax.sharding import PartitionSpec as P

HEAD = 104
IMG_W = 16


EPSILON = 1e-06


def normalize_rows(values, gain, bias):
    values = values.astype(jnp.float32)
    center = values - jnp.mean(values, axis=-1, keepdims=True)
    spread = jnp.mean(center * center, axis=-1, keepdims=True)
    return center * lax.rsqrt(spread + EPSILON) * gain + bias


def normalize_from_sums(values, sums, features, gain, bias):
    values = values.astype(jnp.float32)
    row_mean = sums[0] / features
    spread = sums[1] / features - row_mean * row_mean
    return (values - row_mean[:, None]) * lax.rsqrt(spread[:, None] + EPSILON) * gain + bias


def own_slice(vector, width):
    return lax.dynamic_slice_in_dim(vector, lax.axis_index("gx") * width, width, 0)


def row_sums(values):
    values = values.astype(jnp.float32)
    return (jnp.sum(values, axis=-1), jnp.sum(values * values, axis=-1))


def ring_perm(n, shift):
    return [(j, (j + shift) % n) for j in range(n)]


def gx_gather_blocks(x, n):
    me = lax.axis_index("gx")
    half = x.shape[0] // 2
    from_left = lax.ppermute(x, "gx", ring_perm(n, 1))
    from_right = lax.ppermute(x, "gx", ring_perm(n, -1))
    far_top = lax.ppermute(from_left[:half], "gx", ring_perm(n, 1))
    far_bottom = lax.ppermute(from_right[half:], "gx", ring_perm(n, -1))
    far = jnp.concatenate([far_top, far_bottom], axis=0)
    relative = [x, from_right, far, from_left]
    doubled = jnp.stack(relative + relative, axis=1)
    return lax.dynamic_slice_in_dim(doubled, (n - me) % n, n, axis=1)


def gx_all_gather(x, n):
    blocks = gx_gather_blocks(x, n)
    return blocks.reshape(x.shape[0], n * x.shape[1])


def gx_reduce_scatter(y, n):
    me = lax.axis_index("gx")
    rows = y.shape[0]
    width = y.shape[1] // n
    half = rows // 2
    blocks = y.reshape(rows, n, width)

    def own(part, index):
        return lax.dynamic_slice_in_dim(part, index % n, 1, axis=1)[:, 0]

    top = blocks[:half]
    bottom = blocks[half:]
    acc_top = own(top, me - 1)
    acc_bottom = own(bottom, me + 1)
    for step in range(1, n):
        got_top = lax.ppermute(acc_top.astype(jnp.bfloat16), "gx", ring_perm(n, 1))
        got_bottom = lax.ppermute(acc_bottom.astype(jnp.bfloat16), "gx", ring_perm(n, -1))
        acc_top = got_top.astype(jnp.float32) + own(top, me - step - 1)
        acc_bottom = got_bottom.astype(jnp.float32) + own(bottom, me + step + 1)
    return jnp.concatenate([acc_top, acc_bottom], axis=0)


def gx_sum_rows(sums, n):
    blocks = gx_gather_blocks(sums, n)
    total = blocks[:, 0]
    for j in range(1, n):
        total = total + blocks[:, j]
    return total


def local_attention(qkv, segment_ids):
    tok_rows = qkv.shape[1]
    head_count = qkv.shape[2] // HEAD
    queries = qkv[0].reshape(tok_rows, head_count, HEAD)
    key_rows = qkv[1].reshape(tok_rows, head_count, HEAD)
    value_rows = qkv[2].reshape(tok_rows, head_count, HEAD)
    query_block = min(512, tok_rows)

    def one_block(index):
        first_query = index * query_block
        query_part = lax.dynamic_slice_in_dim(queries, first_query, query_block, 0)
        query_ids = lax.dynamic_slice_in_dim(segment_ids, first_query, query_block, 0)
        scores = jnp.einsum(
            "qhe,khe->hqk", query_part, key_rows, preferred_element_type=jnp.float32
        ) * HEAD ** (-0.5)
        same_segment = query_ids[None, :, None] == segment_ids[None, None, :]
        scores = jnp.where(same_segment, scores, -1e30)
        highest = jnp.max(scores, axis=-1, keepdims=True)
        raised = jnp.exp(scores - highest)
        shares = (raised / jnp.sum(raised, axis=-1, keepdims=True)).astype(jnp.bfloat16)
        return jnp.einsum(
            "hqk,khe->qhe", shares, value_rows, preferred_element_type=jnp.float32
        ).astype(jnp.bfloat16)

    blocks = lax.map(one_block, jnp.arange(tok_rows // query_block, dtype=jnp.int32))
    return blocks.reshape(tok_rows, head_count * HEAD)


def body(
    tokens,
    segment_ids,
    first_gain,
    first_bias,
    query_key_value,
    project_out,
    second_gain,
    second_bias,
    up_weight,
    down_weight,
    final_gain,
    final_bias,
    merge_weight,
    owners,
):
    tok_rows = tokens.shape[0]
    feature_cols = tokens.shape[1]
    n_gx = lax.axis_size("gx")
    features = feature_cols * n_gx
    full_rows = gx_all_gather(tokens, n_gx)
    normed = normalize_rows(full_rows, first_gain, first_bias).astype(jnp.bfloat16)
    columns = normed
    qkv = jnp.einsum(
        "td,kdc->ktc",
        columns,
        lax.all_gather(query_key_value, "gy", axis=1, tiled=True),
        preferred_element_type=jnp.float32,
    ).astype(jnp.bfloat16)
    attended = local_attention(qkv, segment_ids)
    out_terms = jnp.dot(
        attended,
        lax.all_gather(project_out, "gy", axis=1, tiled=True),
        preferred_element_type=jnp.float32,
    )
    attn_share = gx_reduce_scatter(out_terms, n_gx)
    first_resid = (tokens.astype(jnp.float32) + attn_share).astype(jnp.bfloat16)
    resid_rows = gx_all_gather(first_resid, n_gx)
    second_normed = normalize_rows(resid_rows, second_gain, second_bias).astype(jnp.bfloat16)
    columns = second_normed
    upper = jnp.dot(
        columns,
        lax.all_gather(up_weight, "gy", axis=0, tiled=True),
        preferred_element_type=jnp.float32,
    )
    hidden = jax.nn.gelu(upper, approximate=False).astype(jnp.bfloat16)
    down_terms = jnp.dot(
        hidden,
        lax.all_gather(down_weight, "gy", axis=1, tiled=True),
        preferred_element_type=jnp.float32,
    )
    mlp_share = gx_reduce_scatter(down_terms, n_gx)
    second_resid = (first_resid.astype(jnp.float32) + mlp_share).astype(jnp.bfloat16)
    post_sums = gx_sum_rows(jnp.stack(row_sums(second_resid)), n_gx)
    final_normed = normalize_from_sums(
        second_resid,
        post_sums,
        features,
        own_slice(final_gain, feature_cols),
        own_slice(final_bias, feature_cols),
    ).astype(jnp.bfloat16)
    merged_rows = tok_rows // 4
    grouped = (
        final_normed.reshape(tok_rows // (2 * IMG_W), 2, IMG_W // 2, 2, feature_cols)
        .transpose(0, 2, 1, 3, 4)
        .reshape(merged_rows, 4, feature_cols)
    )
    merge_terms = jnp.einsum(
        "pkf,kfc->pc",
        grouped,
        lax.all_gather(merge_weight, "gy", axis=2, tiled=True),
        preferred_element_type=jnp.float32,
    )
    projected = gx_reduce_scatter(merge_terms, n_gx).astype(jnp.bfloat16)
    owner_count = lax.axis_size("gy")
    capacity = max(2, 2 * merged_rows // owner_count)
    owner_col = owners[:, 0]
    one_hot = (owner_col[:, None] == jnp.arange(owner_count, dtype=jnp.int32)[None, :]).astype(
        jnp.int32
    )
    slot_rank = jnp.sum((jnp.cumsum(one_hot, axis=0) - 1) * one_hot, axis=1)
    target = jnp.where(slot_rank < capacity, owner_col * capacity + slot_rank, -1)
    picks = (
        target[None, :] == jnp.arange(owner_count * capacity, dtype=jnp.int32)[:, None]
    ).astype(jnp.bfloat16)
    outgoing = jnp.dot(picks, projected, preferred_element_type=jnp.float32).astype(
        jnp.bfloat16
    ).reshape(owner_count, capacity, feature_cols)
    arrived = lax.all_to_all(outgoing, "gy", split_axis=0, concat_axis=0, tiled=True)
    return arrived.reshape(1, owner_count, capacity, feature_cols)


def solution(mesh):
    in_specs = (
        P("gy", "gx"),
        P("gy"),
        P(),
        P(),
        P(None, "gy", "gx"),
        P("gx", "gy"),
        P(),
        P(),
        P("gy", "gx"),
        P("gx", "gy"),
        P(),
        P(),
        P(None, "gx", "gy"),
        P("gy", None),
    )
    out_specs = P("gy", None, None, "gx")
    return jax.shard_map(body, mesh=mesh, in_specs=in_specs, out_specs=out_specs, check_vma=False)
```

```python
import jax
import jax.numpy as jnp
from jax import lax
from jax.sharding import PartitionSpec as P

HEAD = 104
IMG_W = 16


EPSILON = 1e-06


def normalize_rows(values, gain, bias):
    values = values.astype(jnp.float32)
    center = values - jnp.mean(values, axis=-1, keepdims=True)
    spread = jnp.mean(center * center, axis=-1, keepdims=True)
    return center * lax.rsqrt(spread + EPSILON) * gain + bias


def normalize_from_sums(values, sums, features, gain, bias):
    values = values.astype(jnp.float32)
    row_mean = sums[0] / features
    spread = sums[1] / features - row_mean * row_mean
    return (values - row_mean[:, None]) * lax.rsqrt(spread[:, None] + EPSILON) * gain + bias


def own_slice(vector, width):
    return lax.dynamic_slice_in_dim(vector, lax.axis_index("gx") * width, width, 0)


def row_sums(values):
    values = values.astype(jnp.float32)
    return (jnp.sum(values, axis=-1), jnp.sum(values * values, axis=-1))


def ring_perm(n, shift):
    return [(j, (j + shift) % n) for j in range(n)]


def gx_gather_blocks(x, n):
    me = lax.axis_index("gx")
    half = x.shape[0] // 2
    from_left = lax.ppermute(x, "gx", ring_perm(n, 1))
    from_right = lax.ppermute(x, "gx", ring_perm(n, -1))
    far_top = lax.ppermute(from_left[:half], "gx", ring_perm(n, 1))
    far_bottom = lax.ppermute(from_right[half:], "gx", ring_perm(n, -1))
    far = jnp.concatenate([far_top, far_bottom], axis=0)
    relative = [x, from_right, far, from_left]
    doubled = jnp.stack(relative + relative, axis=1)
    return lax.dynamic_slice_in_dim(doubled, (n - me) % n, n, axis=1)


def gx_all_gather(x, n):
    blocks = gx_gather_blocks(x, n)
    return blocks.reshape(x.shape[0], n * x.shape[1])


def gx_reduce_scatter(y, n):
    me = lax.axis_index("gx")
    rows = y.shape[0]
    width = y.shape[1] // n
    half = rows // 2
    blocks = y.reshape(rows, n, width)

    def own(part, index):
        return lax.dynamic_slice_in_dim(part, index % n, 1, axis=1)[:, 0]

    top = blocks[:half]
    bottom = blocks[half:]
    acc_top = own(top, me - 1)
    acc_bottom = own(bottom, me + 1)
    for step in range(1, n):
        got_top = lax.ppermute(acc_top.astype(jnp.bfloat16), "gx", ring_perm(n, 1))
        got_bottom = lax.ppermute(acc_bottom.astype(jnp.bfloat16), "gx", ring_perm(n, -1))
        acc_top = got_top.astype(jnp.float32) + own(top, me - step - 1)
        acc_bottom = got_bottom.astype(jnp.float32) + own(bottom, me + step + 1)
    return jnp.concatenate([acc_top, acc_bottom], axis=0)


def gx_sum_rows(sums, n):
    blocks = gx_gather_blocks(sums, n)
    total = blocks[:, 0]
    for j in range(1, n):
        total = total + blocks[:, j]
    return total


def local_attention(qkv, segment_ids):
    tok_rows = qkv.shape[1]
    head_count = qkv.shape[2] // HEAD
    queries = qkv[0].reshape(tok_rows, head_count, HEAD)
    key_rows = qkv[1].reshape(tok_rows, head_count, HEAD)
    value_rows = qkv[2].reshape(tok_rows, head_count, HEAD)
    query_block = min(512, tok_rows)

    def one_block(index):
        first_query = index * query_block
        query_part = lax.dynamic_slice_in_dim(queries, first_query, query_block, 0)
        query_ids = lax.dynamic_slice_in_dim(segment_ids, first_query, query_block, 0)
        scores = jnp.einsum(
            "qhe,khe->hqk", query_part, key_rows, preferred_element_type=jnp.float32
        ) * HEAD ** (-0.5)
        same_segment = query_ids[None, :, None] == segment_ids[None, None, :]
        scores = jnp.where(same_segment, scores, -1e30)
        highest = jnp.max(scores, axis=-1, keepdims=True)
        raised = jnp.exp(scores - highest)
        shares = (raised / jnp.sum(raised, axis=-1, keepdims=True)).astype(jnp.bfloat16)
        return jnp.einsum(
            "hqk,khe->qhe", shares, value_rows, preferred_element_type=jnp.float32
        ).astype(jnp.bfloat16)

    blocks = lax.map(one_block, jnp.arange(tok_rows // query_block, dtype=jnp.int32))
    return blocks.reshape(tok_rows, head_count * HEAD)


def body(
    tokens,
    segment_ids,
    first_gain,
    first_bias,
    query_key_value,
    project_out,
    second_gain,
    second_bias,
    up_weight,
    down_weight,
    final_gain,
    final_bias,
    merge_weight,
    owners,
):
    tok_rows = tokens.shape[0]
    feature_cols = tokens.shape[1]
    n_gx = lax.axis_size("gx")
    features = feature_cols * n_gx
    qkv_local = query_key_value
    proj_local = project_out
    first_pack = jnp.concatenate([qkv_local.reshape(1, -1), proj_local.reshape(1, -1)], axis=1)
    first_all = lax.all_gather(first_pack, "gy", axis=0, tiled=True)
    n_gy = first_all.shape[0]
    qkv_size = qkv_local.size
    qkv_all = (
        first_all[:, :qkv_size]
        .reshape((n_gy,) + qkv_local.shape)
        .transpose(1, 0, 2, 3)
        .reshape(qkv_local.shape[0], n_gy * qkv_local.shape[1], qkv_local.shape[2])
    )
    proj_all = (
        first_all[:, qkv_size:]
        .reshape((n_gy,) + proj_local.shape)
        .transpose(1, 0, 2)
        .reshape(proj_local.shape[0], n_gy * proj_local.shape[1])
    )
    up_local, down_local, merge_local = up_weight, down_weight, merge_weight
    second_pack = jnp.concatenate(
        [up_local.reshape(1, -1), down_local.reshape(1, -1), merge_local.reshape(1, -1)], axis=1
    )
    second_pack, _ = lax.optimization_barrier((second_pack, first_all))
    second_all = lax.all_gather(second_pack, "gy", axis=0, tiled=True)
    up_end = up_local.size
    down_end = up_end + down_local.size
    up_all = second_all[:, :up_end].reshape(n_gy * up_local.shape[0], up_local.shape[1])
    down_all = (
        second_all[:, up_end:down_end]
        .reshape((n_gy,) + down_local.shape)
        .transpose(1, 0, 2)
        .reshape(down_local.shape[0], n_gy * down_local.shape[1])
    )
    merge_all = (
        second_all[:, down_end:]
        .reshape((n_gy,) + merge_local.shape)
        .transpose(1, 2, 0, 3)
        .reshape(merge_local.shape[0], merge_local.shape[1], n_gy * merge_local.shape[2])
    )
    full_rows = gx_all_gather(tokens, n_gx)
    normed = normalize_rows(full_rows, first_gain, first_bias).astype(jnp.bfloat16)
    columns = normed
    qkv = jnp.einsum(
        "td,kdc->ktc",
        columns,
        qkv_all,
        preferred_element_type=jnp.float32,
    ).astype(jnp.bfloat16)
    attended = local_attention(qkv, segment_ids)
    out_terms = jnp.dot(
        attended,
        proj_all,
        preferred_element_type=jnp.float32,
    )
    attn_share = gx_reduce_scatter(out_terms, n_gx)
    first_resid = (tokens.astype(jnp.float32) + attn_share).astype(jnp.bfloat16)
    resid_rows = gx_all_gather(first_resid, n_gx)
    second_normed = normalize_rows(resid_rows, second_gain, second_bias).astype(jnp.bfloat16)
    columns = second_normed
    upper = jnp.dot(
        columns,
        up_all,
        preferred_element_type=jnp.float32,
    )
    hidden = jax.nn.gelu(upper, approximate=False).astype(jnp.bfloat16)
    hidden = lax.optimization_barrier(hidden)
    down_terms = jnp.dot(
        hidden,
        down_all,
        preferred_element_type=jnp.float32,
    )
    mlp_share = gx_reduce_scatter(down_terms, n_gx)
    second_resid = (first_resid.astype(jnp.float32) + mlp_share).astype(jnp.bfloat16)
    post_sums = gx_sum_rows(jnp.stack(row_sums(second_resid)), n_gx)
    final_normed = normalize_from_sums(
        second_resid,
        post_sums,
        features,
        own_slice(final_gain, feature_cols),
        own_slice(final_bias, feature_cols),
    ).astype(jnp.bfloat16)
    merged_rows = tok_rows // 4
    grouped = (
        final_normed.reshape(tok_rows // (2 * IMG_W), 2, IMG_W // 2, 2, feature_cols)
        .transpose(0, 2, 1, 3, 4)
        .reshape(merged_rows, 4, feature_cols)
    )
    merge_terms = jnp.einsum(
        "pkf,kfc->pc",
        grouped,
        merge_all,
        preferred_element_type=jnp.float32,
    )
    projected = gx_reduce_scatter(merge_terms, n_gx).astype(jnp.bfloat16)
    owner_count = lax.axis_size("gy")
    capacity = max(2, 2 * merged_rows // owner_count)
    owner_col = owners[:, 0]
    one_hot = (owner_col[:, None] == jnp.arange(owner_count, dtype=jnp.int32)[None, :]).astype(
        jnp.int32
    )
    slot_rank = jnp.sum((jnp.cumsum(one_hot, axis=0) - 1) * one_hot, axis=1)
    target = jnp.where(slot_rank < capacity, owner_col * capacity + slot_rank, -1)
    picks = (
        target[None, :] == jnp.arange(owner_count * capacity, dtype=jnp.int32)[:, None]
    ).astype(jnp.bfloat16)
    outgoing = jnp.dot(picks, projected, preferred_element_type=jnp.float32).astype(
        jnp.bfloat16
    ).reshape(owner_count, capacity, feature_cols)
    arrived = lax.all_to_all(outgoing, "gy", split_axis=0, concat_axis=0, tiled=True)
    return arrived.reshape(1, owner_count, capacity, feature_cols)


def solution(mesh):
    in_specs = (
        P("gy", "gx"),
        P("gy"),
        P(),
        P(),
        P(None, "gy", "gx"),
        P("gx", "gy"),
        P(),
        P(),
        P("gy", "gx"),
        P("gx", "gy"),
        P(),
        P(),
        P(None, "gx", "gy"),
        P("gy", None),
    )
    out_specs = P("gy", None, None, "gx")
    return jax.shard_map(body, mesh=mesh, in_specs=in_specs, out_specs=out_specs, check_vma=False)
```

```python
import jax
import jax.numpy as jnp
from jax import lax
from jax.sharding import PartitionSpec as P

HEAD = 104
IMG_W = 16


EPSILON = 1e-06


def normalize_rows(values, gain, bias):
    values = values.astype(jnp.float32)
    center = values - jnp.mean(values, axis=-1, keepdims=True)
    spread = jnp.mean(center * center, axis=-1, keepdims=True)
    return center * lax.rsqrt(spread + EPSILON) * gain + bias


def normalize_from_sums(values, sums, features, gain, bias):
    values = values.astype(jnp.float32)
    row_mean = sums[0] / features
    spread = sums[1] / features - row_mean * row_mean
    return (values - row_mean[:, None]) * lax.rsqrt(spread[:, None] + EPSILON) * gain + bias


def own_slice(vector, width):
    return lax.dynamic_slice_in_dim(vector, lax.axis_index("gx") * width, width, 0)


def row_sums(values):
    values = values.astype(jnp.float32)
    return (jnp.sum(values, axis=-1), jnp.sum(values * values, axis=-1))


def ring_perm(n, shift):
    return [(j, (j + shift) % n) for j in range(n)]


def gx_gather_blocks(x, n):
    me = lax.axis_index("gx")
    half = x.shape[0] // 2
    from_left = lax.ppermute(x, "gx", ring_perm(n, 1))
    from_right = lax.ppermute(x, "gx", ring_perm(n, -1))
    far_top = lax.ppermute(from_left[:half], "gx", ring_perm(n, 1))
    far_bottom = lax.ppermute(from_right[half:], "gx", ring_perm(n, -1))
    far = jnp.concatenate([far_top, far_bottom], axis=0)
    relative = [x, from_right, far, from_left]
    doubled = jnp.stack(relative + relative, axis=1)
    return lax.dynamic_slice_in_dim(doubled, (n - me) % n, n, axis=1)


def gx_all_gather(x, n):
    blocks = gx_gather_blocks(x, n)
    return blocks.reshape(x.shape[0], n * x.shape[1])


def gx_reduce_scatter(y, n):
    me = lax.axis_index("gx")
    rows = y.shape[0]
    width = y.shape[1] // n
    half = rows // 2
    blocks = y.reshape(rows, n, width)

    def own(part, index):
        return lax.dynamic_slice_in_dim(part, index % n, 1, axis=1)[:, 0]

    top = blocks[:half]
    bottom = blocks[half:]
    acc_top = own(top, me - 1)
    acc_bottom = own(bottom, me + 1)
    for step in range(1, n):
        got_top = lax.ppermute(acc_top.astype(jnp.bfloat16), "gx", ring_perm(n, 1))
        got_bottom = lax.ppermute(acc_bottom.astype(jnp.bfloat16), "gx", ring_perm(n, -1))
        acc_top = got_top.astype(jnp.float32) + own(top, me - step - 1)
        acc_bottom = got_bottom.astype(jnp.float32) + own(bottom, me + step + 1)
    return jnp.concatenate([acc_top, acc_bottom], axis=0)


def gx_sum_rows(sums, n):
    blocks = gx_gather_blocks(sums, n)
    total = blocks[:, 0]
    for j in range(1, n):
        total = total + blocks[:, j]
    return total


def local_attention(qkv, segment_ids):
    tok_rows = qkv.shape[1]
    head_count = qkv.shape[2] // HEAD
    queries = qkv[0].reshape(tok_rows, head_count, HEAD)
    key_rows = qkv[1].reshape(tok_rows, head_count, HEAD)
    value_rows = qkv[2].reshape(tok_rows, head_count, HEAD)
    query_block = min(512, tok_rows)

    def one_block(index):
        first_query = index * query_block
        query_part = lax.dynamic_slice_in_dim(queries, first_query, query_block, 0)
        query_ids = lax.dynamic_slice_in_dim(segment_ids, first_query, query_block, 0)
        scores = jnp.einsum(
            "qhe,khe->hqk", query_part, key_rows, preferred_element_type=jnp.float32
        ) * HEAD ** (-0.5)
        same_segment = query_ids[None, :, None] == segment_ids[None, None, :]
        scores = jnp.where(same_segment, scores, -1e30)
        highest = jnp.max(scores, axis=-1, keepdims=True)
        raised = jnp.exp(scores - highest)
        shares = (raised / jnp.sum(raised, axis=-1, keepdims=True)).astype(jnp.bfloat16)
        return jnp.einsum(
            "hqk,khe->qhe", shares, value_rows, preferred_element_type=jnp.float32
        ).astype(jnp.bfloat16)

    blocks = lax.map(one_block, jnp.arange(tok_rows // query_block, dtype=jnp.int32))
    return blocks.reshape(tok_rows, head_count * HEAD)


def body(
    tokens,
    segment_ids,
    first_gain,
    first_bias,
    query_key_value,
    project_out,
    second_gain,
    second_bias,
    up_weight,
    down_weight,
    final_gain,
    final_bias,
    merge_weight,
    owners,
):
    tok_rows = tokens.shape[0]
    feature_cols = tokens.shape[1]
    n_gx = lax.axis_size("gx")
    features = feature_cols * n_gx
    qkv_all = lax.all_gather(query_key_value, "gy", axis=1, tiled=True)
    proj_all = lax.all_gather(project_out, "gy", axis=1, tiled=True)
    up_all = lax.all_gather(up_weight, "gy", axis=0, tiled=True)
    down_all = lax.all_gather(down_weight, "gy", axis=1, tiled=True)
    merge_all = lax.all_gather(merge_weight, "gy", axis=2, tiled=True)
    full_rows = gx_all_gather(tokens, n_gx)
    normed = normalize_rows(full_rows, first_gain, first_bias).astype(jnp.bfloat16)
    columns = normed
    qkv = jnp.einsum(
        "td,kdc->ktc",
        columns,
        qkv_all,
        preferred_element_type=jnp.float32,
    ).astype(jnp.bfloat16)
    attended = local_attention(qkv, segment_ids)
    out_terms = jnp.dot(
        attended,
        proj_all,
        preferred_element_type=jnp.float32,
    )
    attn_share = gx_reduce_scatter(out_terms, n_gx)
    first_resid = (tokens.astype(jnp.float32) + attn_share).astype(jnp.bfloat16)
    resid_rows = gx_all_gather(first_resid, n_gx)
    second_normed = normalize_rows(resid_rows, second_gain, second_bias).astype(jnp.bfloat16)
    columns = second_normed
    upper = jnp.dot(
        columns,
        up_all,
        preferred_element_type=jnp.float32,
    )
    hidden = jax.nn.gelu(upper, approximate=False).astype(jnp.bfloat16)
    down_terms = jnp.dot(
        hidden,
        down_all,
        preferred_element_type=jnp.float32,
    )
    mlp_share = gx_reduce_scatter(down_terms, n_gx)
    second_resid = (first_resid.astype(jnp.float32) + mlp_share).astype(jnp.bfloat16)
    post_sums = gx_sum_rows(jnp.stack(row_sums(second_resid)), n_gx)
    final_normed = normalize_from_sums(
        second_resid,
        post_sums,
        features,
        own_slice(final_gain, feature_cols),
        own_slice(final_bias, feature_cols),
    ).astype(jnp.bfloat16)
    merged_rows = tok_rows // 4
    grouped = (
        final_normed.reshape(tok_rows // (2 * IMG_W), 2, IMG_W // 2, 2, feature_cols)
        .transpose(0, 2, 1, 3, 4)
        .reshape(merged_rows, 4, feature_cols)
    )
    merge_terms = jnp.einsum(
        "pkf,kfc->pc",
        grouped,
        merge_all,
        preferred_element_type=jnp.float32,
    )
    projected = gx_reduce_scatter(merge_terms, n_gx).astype(jnp.bfloat16)
    owner_count = lax.axis_size("gy")
    capacity = max(2, 2 * merged_rows // owner_count)
    owner_col = owners[:, 0]
    one_hot = (owner_col[:, None] == jnp.arange(owner_count, dtype=jnp.int32)[None, :]).astype(
        jnp.int32
    )
    slot_rank = jnp.sum((jnp.cumsum(one_hot, axis=0) - 1) * one_hot, axis=1)
    target = jnp.where(slot_rank < capacity, owner_col * capacity + slot_rank, -1)
    picks = (
        target[None, :] == jnp.arange(owner_count * capacity, dtype=jnp.int32)[:, None]
    ).astype(jnp.bfloat16)
    outgoing = jnp.dot(picks, projected, preferred_element_type=jnp.float32).astype(
        jnp.bfloat16
    ).reshape(owner_count, capacity, feature_cols)
    arrived = lax.all_to_all(outgoing, "gy", split_axis=0, concat_axis=0, tiled=True)
    return arrived.reshape(1, owner_count, capacity, feature_cols)


def solution(mesh):
    in_specs = (
        P("gy", "gx"),
        P("gy"),
        P(),
        P(),
        P(None, "gy", "gx"),
        P("gx", "gy"),
        P(),
        P(),
        P("gy", "gx"),
        P("gx", "gy"),
        P(),
        P(),
        P(None, "gx", "gy"),
        P("gy", None),
    )
    out_specs = P("gy", None, None, "gx")

    return jax.shard_map(body, mesh=mesh, in_specs=in_specs, out_specs=out_specs, check_vma=False)
```

```python
import jax
import jax.numpy as jnp
from jax import lax
from jax.sharding import PartitionSpec as P

HEAD = 104
IMG_W = 16


EPSILON = 1e-06


def normalize_rows(values, gain, bias):
    values = values.astype(jnp.float32)
    center = values - jnp.mean(values, axis=-1, keepdims=True)
    spread = jnp.mean(center * center, axis=-1, keepdims=True)
    return center * lax.rsqrt(spread + EPSILON) * gain + bias


def normalize_from_sums(values, sums, features, gain, bias):
    values = values.astype(jnp.float32)
    row_mean = sums[0] / features
    spread = sums[1] / features - row_mean * row_mean
    return (values - row_mean[:, None]) * lax.rsqrt(spread[:, None] + EPSILON) * gain + bias


def own_slice(vector, width):
    return lax.dynamic_slice_in_dim(vector, lax.axis_index("gx") * width, width, 0)


def row_sums(values):
    values = values.astype(jnp.float32)
    return (jnp.sum(values, axis=-1), jnp.sum(values * values, axis=-1))


def ring_perm(n, shift):
    return [(j, (j + shift) % n) for j in range(n)]


def gx_gather_blocks(x, n):
    me = lax.axis_index("gx")
    half = x.shape[0] // 2
    from_left = lax.ppermute(x, "gx", ring_perm(n, 1))
    from_right = lax.ppermute(x, "gx", ring_perm(n, -1))
    far_top = lax.ppermute(from_left[:half], "gx", ring_perm(n, 1))
    far_bottom = lax.ppermute(from_right[half:], "gx", ring_perm(n, -1))
    far = jnp.concatenate([far_top, far_bottom], axis=0)
    relative = [x, from_right, far, from_left]
    doubled = jnp.stack(relative + relative, axis=1)
    return lax.dynamic_slice_in_dim(doubled, (n - me) % n, n, axis=1)


def gx_all_gather(x, n):
    blocks = gx_gather_blocks(x, n)
    return blocks.reshape(x.shape[0], n * x.shape[1])


def gx_reduce_scatter(y, n):
    me = lax.axis_index("gx")
    rows = y.shape[0]
    width = y.shape[1] // n
    half = rows // 2
    blocks = y.reshape(rows, n, width)

    def own(part, index):
        return lax.dynamic_slice_in_dim(part, index % n, 1, axis=1)[:, 0]

    top = blocks[:half]
    bottom = blocks[half:]
    acc_top = own(top, me - 1)
    acc_bottom = own(bottom, me + 1)
    for step in range(1, n):
        got_top = lax.ppermute(acc_top.astype(jnp.bfloat16), "gx", ring_perm(n, 1))
        got_bottom = lax.ppermute(acc_bottom.astype(jnp.bfloat16), "gx", ring_perm(n, -1))
        acc_top = got_top.astype(jnp.float32) + own(top, me - step - 1)
        acc_bottom = got_bottom.astype(jnp.float32) + own(bottom, me + step + 1)
    return jnp.concatenate([acc_top, acc_bottom], axis=0)


def gx_sum_rows(sums, n):
    blocks = gx_gather_blocks(sums, n)
    total = blocks[:, 0]
    for j in range(1, n):
        total = total + blocks[:, j]
    return total


def local_attention(qkv, segment_ids):
    tok_rows = qkv.shape[1]
    head_count = qkv.shape[2] // HEAD
    queries = qkv[0].reshape(tok_rows, head_count, HEAD)
    key_rows = qkv[1].reshape(tok_rows, head_count, HEAD)
    value_rows = qkv[2].reshape(tok_rows, head_count, HEAD)
    query_block = min(512, tok_rows)

    def one_block(index):
        first_query = index * query_block
        query_part = lax.dynamic_slice_in_dim(queries, first_query, query_block, 0)
        query_ids = lax.dynamic_slice_in_dim(segment_ids, first_query, query_block, 0)
        scores = jnp.einsum(
            "qhe,khe->hqk", query_part, key_rows, preferred_element_type=jnp.float32
        ) * HEAD ** (-0.5)
        same_segment = query_ids[None, :, None] == segment_ids[None, None, :]
        scores = jnp.where(same_segment, scores, -1e30)
        highest = jnp.max(scores, axis=-1, keepdims=True)
        raised = jnp.exp(scores - highest)
        shares = (raised / jnp.sum(raised, axis=-1, keepdims=True)).astype(jnp.bfloat16)
        return jnp.einsum(
            "hqk,khe->qhe", shares, value_rows, preferred_element_type=jnp.float32
        ).astype(jnp.bfloat16)

    blocks = lax.map(one_block, jnp.arange(tok_rows // query_block, dtype=jnp.int32))
    return blocks.reshape(tok_rows, head_count * HEAD)


def post_attention(attended, tokens, proj_all, up_all, down_all, merge_all,
                   second_gain, second_bias, final_gain, final_bias, n_gx, features):
    tok_rows = tokens.shape[0]
    feature_cols = tokens.shape[1]
    out_terms = jnp.dot(
        attended,
        proj_all,
        preferred_element_type=jnp.float32,
    )
    attn_share = gx_reduce_scatter(out_terms, n_gx)
    first_resid = (tokens.astype(jnp.float32) + attn_share).astype(jnp.bfloat16)
    resid_rows = gx_all_gather(first_resid, n_gx)
    second_normed = normalize_rows(resid_rows, second_gain, second_bias).astype(jnp.bfloat16)
    columns = second_normed
    upper = jnp.dot(
        columns,
        up_all,
        preferred_element_type=jnp.float32,
    )
    hidden = jax.nn.gelu(upper, approximate=False).astype(jnp.bfloat16)
    down_terms = jnp.dot(
        hidden,
        down_all,
        preferred_element_type=jnp.float32,
    )
    mlp_share = gx_reduce_scatter(down_terms, n_gx)
    second_resid = (first_resid.astype(jnp.float32) + mlp_share).astype(jnp.bfloat16)
    post_sums = gx_sum_rows(jnp.stack(row_sums(second_resid)), n_gx)
    final_normed = normalize_from_sums(
        second_resid,
        post_sums,
        features,
        own_slice(final_gain, feature_cols),
        own_slice(final_bias, feature_cols),
    ).astype(jnp.bfloat16)
    merged_rows = tok_rows // 4
    grouped = (
        final_normed.reshape(tok_rows // (2 * IMG_W), 2, IMG_W // 2, 2, feature_cols)
        .transpose(0, 2, 1, 3, 4)
        .reshape(merged_rows, 4, feature_cols)
    )
    merge_terms = jnp.einsum(
        "pkf,kfc->pc",
        grouped,
        merge_all,
        preferred_element_type=jnp.float32,
    )
    projected = gx_reduce_scatter(merge_terms, n_gx).astype(jnp.bfloat16)
    return projected


def body(
    tokens,
    segment_ids,
    first_gain,
    first_bias,
    query_key_value,
    project_out,
    second_gain,
    second_bias,
    up_weight,
    down_weight,
    final_gain,
    final_bias,
    merge_weight,
    owners,
):
    tok_rows = tokens.shape[0]
    feature_cols = tokens.shape[1]
    n_gx = lax.axis_size("gx")
    features = feature_cols * n_gx
    qkv_all = lax.all_gather(query_key_value, "gy", axis=1, tiled=True)
    proj_all = lax.all_gather(project_out, "gy", axis=1, tiled=True)
    up_all = lax.all_gather(up_weight, "gy", axis=0, tiled=True)
    down_all = lax.all_gather(down_weight, "gy", axis=1, tiled=True)
    merge_all = lax.all_gather(merge_weight, "gy", axis=2, tiled=True)
    full_rows = gx_all_gather(tokens, n_gx)
    normed = normalize_rows(full_rows, first_gain, first_bias).astype(jnp.bfloat16)
    columns = normed
    qkv = jnp.einsum(
        "td,kdc->ktc",
        columns,
        qkv_all,
        preferred_element_type=jnp.float32,
    ).astype(jnp.bfloat16)
    attended = local_attention(qkv, segment_ids)
    chunks = 2
    chunk_rows = tok_rows // chunks
    projected_parts = []
    for chunk in range(chunks):
        rows = slice(chunk * chunk_rows, (chunk + 1) * chunk_rows)
        projected_parts.append(
            post_attention(
                attended[rows], tokens[rows], proj_all, up_all, down_all, merge_all,
                second_gain, second_bias, final_gain, final_bias, n_gx, features,
            )
        )
    projected = jnp.concatenate(projected_parts, axis=0)
    merged_rows = tok_rows // 4
    owner_count = lax.axis_size("gy")
    capacity = max(2, 2 * merged_rows // owner_count)
    owner_col = owners[:, 0]
    one_hot = (owner_col[:, None] == jnp.arange(owner_count, dtype=jnp.int32)[None, :]).astype(
        jnp.int32
    )
    slot_rank = jnp.sum((jnp.cumsum(one_hot, axis=0) - 1) * one_hot, axis=1)
    target = jnp.where(slot_rank < capacity, owner_col * capacity + slot_rank, -1)
    picks = (
        target[None, :] == jnp.arange(owner_count * capacity, dtype=jnp.int32)[:, None]
    ).astype(jnp.bfloat16)
    outgoing = jnp.dot(picks, projected, preferred_element_type=jnp.float32).astype(
        jnp.bfloat16
    ).reshape(owner_count, capacity, feature_cols)
    arrived = lax.all_to_all(outgoing, "gy", split_axis=0, concat_axis=0, tiled=True)
    return arrived.reshape(1, owner_count, capacity, feature_cols)


def solution(mesh):
    in_specs = (
        P("gy", "gx"),
        P("gy"),
        P(),
        P(),
        P(None, "gy", "gx"),
        P("gx", "gy"),
        P(),
        P(),
        P("gy", "gx"),
        P("gx", "gy"),
        P(),
        P(),
        P(None, "gx", "gy"),
        P("gy", None),
    )
    out_specs = P("gy", None, None, "gx")

    return jax.shard_map(body, mesh=mesh, in_specs=in_specs, out_specs=out_specs, check_vma=False)
```

```python
import jax
import jax.numpy as jnp
from jax import lax
from jax.sharding import PartitionSpec as P

HEAD = 104
IMG_W = 16


EPSILON = 1e-06


def normalize_rows(values, gain, bias):
    values = values.astype(jnp.float32)
    center = values - jnp.mean(values, axis=-1, keepdims=True)
    spread = jnp.mean(center * center, axis=-1, keepdims=True)
    return center * lax.rsqrt(spread + EPSILON) * gain + bias


def normalize_from_sums(values, sums, features, gain, bias):
    values = values.astype(jnp.float32)
    row_mean = sums[0] / features
    spread = sums[1] / features - row_mean * row_mean
    return (values - row_mean[:, None]) * lax.rsqrt(spread[:, None] + EPSILON) * gain + bias


def own_slice(vector, width):
    return lax.dynamic_slice_in_dim(vector, lax.axis_index("gx") * width, width, 0)


def row_sums(values):
    values = values.astype(jnp.float32)
    return (jnp.sum(values, axis=-1), jnp.sum(values * values, axis=-1))


def ring_perm(n, shift):
    return [(j, (j + shift) % n) for j in range(n)]


def gx_gather_blocks(x, n):
    me = lax.axis_index("gx")
    half = x.shape[0] // 2
    from_left = lax.ppermute(x, "gx", ring_perm(n, 1))
    from_right = lax.ppermute(x, "gx", ring_perm(n, -1))
    far_top = lax.ppermute(from_left[:half], "gx", ring_perm(n, 1))
    far_bottom = lax.ppermute(from_right[half:], "gx", ring_perm(n, -1))
    far = jnp.concatenate([far_top, far_bottom], axis=0)
    relative = [x, from_right, far, from_left]
    doubled = jnp.stack(relative + relative, axis=1)
    return lax.dynamic_slice_in_dim(doubled, (n - me) % n, n, axis=1)


def gx_all_gather(x, n):
    blocks = gx_gather_blocks(x, n)
    return blocks.reshape(x.shape[0], n * x.shape[1])


def gx_matmul_reduce_scatter(lhs, w_blocks, contract, n):
    me = lax.axis_index("gx")
    half = lhs.shape[0] // 2
    top = lhs[:half]
    bottom = lhs[half:]

    def block(index):
        return lax.dynamic_index_in_dim(w_blocks, index % n, 0, keepdims=False)

    acc_top = contract(top, block(me - 1))
    acc_bottom = contract(bottom, block(me + 1))
    for step in range(1, n):
        got_top = lax.ppermute(acc_top.astype(jnp.bfloat16), "gx", ring_perm(n, 1))
        got_bottom = lax.ppermute(acc_bottom.astype(jnp.bfloat16), "gx", ring_perm(n, -1))
        acc_top = got_top.astype(jnp.float32) + contract(top, block(me - step - 1))
        acc_bottom = got_bottom.astype(jnp.float32) + contract(bottom, block(me + step + 1))
    return jnp.concatenate([acc_top, acc_bottom], axis=0)


def plain_dot(lhs, rhs):
    return jnp.dot(lhs, rhs, preferred_element_type=jnp.float32)


def merge_dot(lhs, rhs):
    return jnp.einsum("pkf,kfc->pc", lhs, rhs, preferred_element_type=jnp.float32)


def gx_sum_rows(sums, n):
    me = lax.axis_index("gx")
    relative = [sums] + [lax.ppermute(sums, "gx", ring_perm(n, -shift)) for shift in range(1, n)]
    doubled = jnp.stack(relative + relative, axis=1)
    blocks = lax.dynamic_slice_in_dim(doubled, (n - me) % n, n, axis=1)
    total = blocks[:, 0]
    for j in range(1, n):
        total = total + blocks[:, j]
    return total


def local_attention(qkv, segment_ids):
    tok_rows = qkv.shape[1]
    head_count = qkv.shape[2] // HEAD
    queries = qkv[0].reshape(tok_rows, head_count, HEAD)
    key_rows = qkv[1].reshape(tok_rows, head_count, HEAD)
    value_rows = qkv[2].reshape(tok_rows, head_count, HEAD)
    query_block = min(512, tok_rows)

    def one_block(index):
        first_query = index * query_block
        query_part = lax.dynamic_slice_in_dim(queries, first_query, query_block, 0)
        query_ids = lax.dynamic_slice_in_dim(segment_ids, first_query, query_block, 0)
        scores = jnp.einsum(
            "qhe,khe->hqk", query_part, key_rows, preferred_element_type=jnp.float32
        ) * HEAD ** (-0.5)
        same_segment = query_ids[None, :, None] == segment_ids[None, None, :]
        scores = jnp.where(same_segment, scores, -1e30)
        highest = jnp.max(scores, axis=-1, keepdims=True)
        raised = jnp.exp(scores - highest)
        shares = (raised / jnp.sum(raised, axis=-1, keepdims=True)).astype(jnp.bfloat16)
        return jnp.einsum(
            "hqk,khe->qhe", shares, value_rows, preferred_element_type=jnp.float32
        ).astype(jnp.bfloat16)

    blocks = lax.map(one_block, jnp.arange(tok_rows // query_block, dtype=jnp.int32))
    return blocks.reshape(tok_rows, head_count * HEAD)


def body(
    tokens,
    segment_ids,
    first_gain,
    first_bias,
    query_key_value,
    project_out,
    second_gain,
    second_bias,
    up_weight,
    down_weight,
    final_gain,
    final_bias,
    merge_weight,
    owners,
):
    tok_rows = tokens.shape[0]
    feature_cols = tokens.shape[1]
    n_gx = lax.axis_size("gx")
    features = feature_cols * n_gx
    qkv_all = lax.all_gather(query_key_value, "gy", axis=1, tiled=True)
    proj_all = lax.all_gather(project_out, "gy", axis=1, tiled=True)
    up_all = lax.all_gather(up_weight, "gy", axis=0, tiled=True)
    down_all = lax.all_gather(down_weight, "gy", axis=1, tiled=True)
    merge_all = lax.all_gather(merge_weight, "gy", axis=2, tiled=True)
    width = feature_cols
    proj_blocks = proj_all.reshape(proj_all.shape[0], n_gx, width).transpose(1, 0, 2)
    down_blocks = down_all.reshape(down_all.shape[0], n_gx, width).transpose(1, 0, 2)
    merge_blocks = merge_all.reshape(
        merge_all.shape[0], merge_all.shape[1], n_gx, width
    ).transpose(2, 0, 1, 3)
    full_rows = gx_all_gather(tokens, n_gx)
    normed = normalize_rows(full_rows, first_gain, first_bias).astype(jnp.bfloat16)
    columns = normed
    qkv = jnp.einsum(
        "td,kdc->ktc",
        columns,
        qkv_all,
        preferred_element_type=jnp.float32,
    ).astype(jnp.bfloat16)
    attended = local_attention(qkv, segment_ids)
    attn_share = gx_matmul_reduce_scatter(attended, proj_blocks, plain_dot, n_gx)
    first_resid = (tokens.astype(jnp.float32) + attn_share).astype(jnp.bfloat16)
    resid_rows = gx_all_gather(first_resid, n_gx)
    second_normed = normalize_rows(resid_rows, second_gain, second_bias).astype(jnp.bfloat16)
    columns = second_normed
    upper = jnp.dot(
        columns,
        up_all,
        preferred_element_type=jnp.float32,
    )
    hidden = jax.nn.gelu(upper, approximate=False).astype(jnp.bfloat16)
    mlp_share = gx_matmul_reduce_scatter(hidden, down_blocks, plain_dot, n_gx)
    second_resid = (first_resid.astype(jnp.float32) + mlp_share).astype(jnp.bfloat16)
    post_sums = gx_sum_rows(jnp.stack(row_sums(second_resid)), n_gx)
    final_normed = normalize_from_sums(
        second_resid,
        post_sums,
        features,
        own_slice(final_gain, feature_cols),
        own_slice(final_bias, feature_cols),
    ).astype(jnp.bfloat16)
    merged_rows = tok_rows // 4
    grouped = (
        final_normed.reshape(tok_rows // (2 * IMG_W), 2, IMG_W // 2, 2, feature_cols)
        .transpose(0, 2, 1, 3, 4)
        .reshape(merged_rows, 4, feature_cols)
    )
    projected = gx_matmul_reduce_scatter(grouped, merge_blocks, merge_dot, n_gx).astype(
        jnp.bfloat16
    )
    owner_count = lax.axis_size("gy")
    capacity = max(2, 2 * merged_rows // owner_count)
    owner_col = owners[:, 0]
    one_hot = (owner_col[:, None] == jnp.arange(owner_count, dtype=jnp.int32)[None, :]).astype(
        jnp.int32
    )
    slot_rank = jnp.sum((jnp.cumsum(one_hot, axis=0) - 1) * one_hot, axis=1)
    target = jnp.where(slot_rank < capacity, owner_col * capacity + slot_rank, -1)
    picks = (
        target[None, :] == jnp.arange(owner_count * capacity, dtype=jnp.int32)[:, None]
    ).astype(jnp.bfloat16)
    outgoing = jnp.dot(picks, projected, preferred_element_type=jnp.float32).astype(
        jnp.bfloat16
    ).reshape(owner_count, capacity, feature_cols)
    arrived = lax.all_to_all(outgoing, "gy", split_axis=0, concat_axis=0, tiled=True)
    return arrived.reshape(1, owner_count, capacity, feature_cols)


def solution(mesh):
    in_specs = (
        P("gy", "gx"),
        P("gy"),
        P(),
        P(),
        P(None, "gy", "gx"),
        P("gx", "gy"),
        P(),
        P(),
        P("gy", "gx"),
        P("gx", "gy"),
        P(),
        P(),
        P(None, "gx", "gy"),
        P("gy", None),
    )
    out_specs = P("gy", None, None, "gx")

    return jax.shard_map(body, mesh=mesh, in_specs=in_specs, out_specs=out_specs, check_vma=False)
```

```python
import jax
import jax.numpy as jnp
from jax import lax
from jax.sharding import PartitionSpec as P

HEAD = 104
IMG_W = 16


EPSILON = 1e-06


def normalize_rows(values, gain, bias):
    values = values.astype(jnp.float32)
    center = values - jnp.mean(values, axis=-1, keepdims=True)
    spread = jnp.mean(center * center, axis=-1, keepdims=True)
    return center * lax.rsqrt(spread + EPSILON) * gain + bias


def normalize_from_sums(values, sums, features, gain, bias):
    values = values.astype(jnp.float32)
    row_mean = sums[0] / features
    spread = sums[1] / features - row_mean * row_mean
    return (values - row_mean[:, None]) * lax.rsqrt(spread[:, None] + EPSILON) * gain + bias


def own_slice(vector, width):
    return lax.dynamic_slice_in_dim(vector, lax.axis_index("gx") * width, width, 0)


def row_sums(values):
    values = values.astype(jnp.float32)
    return (jnp.sum(values, axis=-1), jnp.sum(values * values, axis=-1))


def ring_perm(n, shift):
    return [(j, (j + shift) % n) for j in range(n)]


def gx_all_gather(x, n):
    me = lax.axis_index("gx")
    half = x.shape[0] // 2
    from_left = lax.ppermute(x, "gx", ring_perm(n, 1))
    from_right = lax.ppermute(x, "gx", ring_perm(n, -1))
    far_top = lax.ppermute(from_left[:half], "gx", ring_perm(n, 1))
    far_bottom = lax.ppermute(from_right[half:], "gx", ring_perm(n, -1))
    far = jnp.concatenate([far_top, far_bottom], axis=0)
    relative = [x, from_right, far, from_left]
    columns = []
    for j in range(n):
        offset = (j - me) % n
        block = relative[n - 1]
        for k in range(n - 2, -1, -1):
            block = jnp.where(offset == k, relative[k], block)
        columns.append(block)
    return jnp.concatenate(columns, axis=1)


def gx_matmul_reduce_scatter(lhs, w_blocks, contract, n):
    me = lax.axis_index("gx")
    half = lhs.shape[0] // 2
    top = lhs[:half]
    bottom = lhs[half:]

    def block(index):
        return lax.dynamic_index_in_dim(w_blocks, index % n, 0, keepdims=False)

    acc_top = contract(top, block(me - 1))
    acc_bottom = contract(bottom, block(me + 1))
    for step in range(1, n):
        got_top = lax.ppermute(acc_top.astype(jnp.bfloat16), "gx", ring_perm(n, 1))
        got_bottom = lax.ppermute(acc_bottom.astype(jnp.bfloat16), "gx", ring_perm(n, -1))
        acc_top = got_top.astype(jnp.float32) + contract(top, block(me - step - 1))
        acc_bottom = got_bottom.astype(jnp.float32) + contract(bottom, block(me + step + 1))
    return jnp.concatenate([acc_top, acc_bottom], axis=0)


def plain_dot(lhs, rhs):
    return jnp.dot(lhs, rhs, preferred_element_type=jnp.float32)


def merge_dot(lhs, rhs):
    return jnp.einsum("pkf,kfc->pc", lhs, rhs, preferred_element_type=jnp.float32)


def gx_sum_rows(sums, n):
    me = lax.axis_index("gx")
    relative = [sums] + [lax.ppermute(sums, "gx", ring_perm(n, -shift)) for shift in range(1, n)]
    doubled = jnp.stack(relative + relative, axis=1)
    blocks = lax.dynamic_slice_in_dim(doubled, (n - me) % n, n, axis=1)
    total = blocks[:, 0]
    for j in range(1, n):
        total = total + blocks[:, j]
    return total


def local_attention(qkv, segment_ids):
    tok_rows = qkv.shape[1]
    head_count = qkv.shape[2] // HEAD
    queries = qkv[0].reshape(tok_rows, head_count, HEAD)
    key_rows = qkv[1].reshape(tok_rows, head_count, HEAD)
    value_rows = qkv[2].reshape(tok_rows, head_count, HEAD)
    query_block = min(512, tok_rows)

    def one_block(index):
        first_query = index * query_block
        query_part = lax.dynamic_slice_in_dim(queries, first_query, query_block, 0)
        query_ids = lax.dynamic_slice_in_dim(segment_ids, first_query, query_block, 0)
        scores = jnp.einsum(
            "qhe,khe->hqk", query_part, key_rows, preferred_element_type=jnp.float32
        ) * HEAD ** (-0.5)
        same_segment = query_ids[None, :, None] == segment_ids[None, None, :]
        scores = jnp.where(same_segment, scores, -1e30)
        highest = jnp.max(scores, axis=-1, keepdims=True)
        raised = jnp.exp(scores - highest)
        shares = (raised / jnp.sum(raised, axis=-1, keepdims=True)).astype(jnp.bfloat16)
        return jnp.einsum(
            "hqk,khe->qhe", shares, value_rows, preferred_element_type=jnp.float32
        ).astype(jnp.bfloat16)

    blocks = lax.map(one_block, jnp.arange(tok_rows // query_block, dtype=jnp.int32))
    return blocks.reshape(tok_rows, head_count * HEAD)


def body(
    tokens,
    segment_ids,
    first_gain,
    first_bias,
    query_key_value,
    project_out,
    second_gain,
    second_bias,
    up_weight,
    down_weight,
    final_gain,
    final_bias,
    merge_weight,
    owners,
):
    tok_rows = tokens.shape[0]
    feature_cols = tokens.shape[1]
    n_gx = lax.axis_size("gx")
    features = feature_cols * n_gx
    qkv_all = lax.all_gather(query_key_value, "gy", axis=1, tiled=True)
    proj_all = lax.all_gather(project_out, "gy", axis=1, tiled=True)
    up_all = lax.all_gather(up_weight, "gy", axis=0, tiled=True)
    down_all = lax.all_gather(down_weight, "gy", axis=1, tiled=True)
    merge_all = lax.all_gather(merge_weight, "gy", axis=2, tiled=True)
    width = feature_cols
    proj_blocks = proj_all.reshape(proj_all.shape[0], n_gx, width).transpose(1, 0, 2)
    down_blocks = down_all.reshape(down_all.shape[0], n_gx, width).transpose(1, 0, 2)
    merge_blocks = merge_all.reshape(
        merge_all.shape[0], merge_all.shape[1], n_gx, width
    ).transpose(2, 0, 1, 3)
    full_rows = gx_all_gather(tokens, n_gx)
    normed = normalize_rows(full_rows, first_gain, first_bias).astype(jnp.bfloat16)
    columns = normed
    qkv = jnp.einsum(
        "td,kdc->ktc",
        columns,
        qkv_all,
        preferred_element_type=jnp.float32,
    ).astype(jnp.bfloat16)
    attended = local_attention(qkv, segment_ids)
    attn_share = gx_matmul_reduce_scatter(attended, proj_blocks, plain_dot, n_gx)
    first_resid = (tokens.astype(jnp.float32) + attn_share).astype(jnp.bfloat16)
    resid_rows = gx_all_gather(first_resid, n_gx)
    second_normed = normalize_rows(resid_rows, second_gain, second_bias).astype(jnp.bfloat16)
    columns = second_normed
    upper = jnp.dot(
        columns,
        up_all,
        preferred_element_type=jnp.float32,
    )
    hidden = jax.nn.gelu(upper, approximate=False).astype(jnp.bfloat16)
    mlp_share = gx_matmul_reduce_scatter(hidden, down_blocks, plain_dot, n_gx)
    second_resid = (first_resid.astype(jnp.float32) + mlp_share).astype(jnp.bfloat16)
    post_sums = gx_sum_rows(jnp.stack(row_sums(second_resid)), n_gx)
    final_normed = normalize_from_sums(
        second_resid,
        post_sums,
        features,
        own_slice(final_gain, feature_cols),
        own_slice(final_bias, feature_cols),
    ).astype(jnp.bfloat16)
    merged_rows = tok_rows // 4
    grouped = (
        final_normed.reshape(tok_rows // (2 * IMG_W), 2, IMG_W // 2, 2, feature_cols)
        .transpose(0, 2, 1, 3, 4)
        .reshape(merged_rows, 4, feature_cols)
    )
    projected = gx_matmul_reduce_scatter(grouped, merge_blocks, merge_dot, n_gx).astype(
        jnp.bfloat16
    )
    owner_count = lax.axis_size("gy")
    capacity = max(2, 2 * merged_rows // owner_count)
    owner_col = owners[:, 0]
    one_hot = (owner_col[:, None] == jnp.arange(owner_count, dtype=jnp.int32)[None, :]).astype(
        jnp.int32
    )
    slot_rank = jnp.sum((jnp.cumsum(one_hot, axis=0) - 1) * one_hot, axis=1)
    target = jnp.where(slot_rank < capacity, owner_col * capacity + slot_rank, -1)
    picks = (
        target[None, :] == jnp.arange(owner_count * capacity, dtype=jnp.int32)[:, None]
    ).astype(jnp.bfloat16)
    outgoing = jnp.dot(picks, projected, preferred_element_type=jnp.float32).astype(
        jnp.bfloat16
    ).reshape(owner_count, capacity, feature_cols)
    arrived = lax.all_to_all(outgoing, "gy", split_axis=0, concat_axis=0, tiled=True)
    return arrived.reshape(1, owner_count, capacity, feature_cols)


def solution(mesh):
    in_specs = (
        P("gy", "gx"),
        P("gy"),
        P(),
        P(),
        P(None, "gy", "gx"),
        P("gx", "gy"),
        P(),
        P(),
        P("gy", "gx"),
        P("gx", "gy"),
        P(),
        P(),
        P(None, "gx", "gy"),
        P("gy", None),
    )
    out_specs = P("gy", None, None, "gx")

    return jax.shard_map(body, mesh=mesh, in_specs=in_specs, out_specs=out_specs, check_vma=False)
```

```python
import jax
import jax.numpy as jnp
from jax import lax
from jax.sharding import PartitionSpec as P

HEAD = 104
IMG_W = 16


EPSILON = 1e-06


def normalize_rows(values, gain, bias):
    values = values.astype(jnp.float32)
    center = values - jnp.mean(values, axis=-1, keepdims=True)
    spread = jnp.mean(center * center, axis=-1, keepdims=True)
    return center * lax.rsqrt(spread + EPSILON) * gain + bias


def normalize_from_sums(values, sums, features, gain, bias):
    values = values.astype(jnp.float32)
    row_mean = sums[0] / features
    spread = sums[1] / features - row_mean * row_mean
    return (values - row_mean[:, None]) * lax.rsqrt(spread[:, None] + EPSILON) * gain + bias


def own_slice(vector, width):
    return lax.dynamic_slice_in_dim(vector, lax.axis_index("gx") * width, width, 0)


def row_sums(values):
    values = values.astype(jnp.float32)
    return (jnp.sum(values, axis=-1), jnp.sum(values * values, axis=-1))


def ring_perm(n, shift):
    return [(j, (j + shift) % n) for j in range(n)]


def gx_all_gather(x, n):
    me = lax.axis_index("gx")
    half = x.shape[0] // 2
    from_left = lax.ppermute(x, "gx", ring_perm(n, 1))
    from_right = lax.ppermute(x, "gx", ring_perm(n, -1))
    far_top = lax.ppermute(from_left[:half], "gx", ring_perm(n, 1))
    far_bottom = lax.ppermute(from_right[half:], "gx", ring_perm(n, -1))
    far = jnp.concatenate([far_top, far_bottom], axis=0)
    relative = [x, from_right, far, from_left]
    columns = []
    for j in range(n):
        offset = (j - me) % n
        block = relative[n - 1]
        for k in range(n - 2, -1, -1):
            block = jnp.where(offset == k, relative[k], block)
        columns.append(block)
    return jnp.concatenate(columns, axis=1)


def gx_reduce_scatter(y, n):
    me = lax.axis_index("gx")
    rows = y.shape[0]
    width = y.shape[1] // n
    half = rows // 2
    blocks = y.reshape(rows, n, width)

    def own(part, index):
        return lax.dynamic_slice_in_dim(part, index % n, 1, axis=1)[:, 0]

    top = blocks[:half]
    bottom = blocks[half:]
    acc_top = own(top, me - 1)
    acc_bottom = own(bottom, me + 1)
    for step in range(1, n):
        got_top = lax.ppermute(acc_top.astype(jnp.bfloat16), "gx", ring_perm(n, 1))
        got_bottom = lax.ppermute(acc_bottom.astype(jnp.bfloat16), "gx", ring_perm(n, -1))
        acc_top = got_top.astype(jnp.float32) + own(top, me - step - 1)
        acc_bottom = got_bottom.astype(jnp.float32) + own(bottom, me + step + 1)
    return jnp.concatenate([acc_top, acc_bottom], axis=0)


def gx_matmul_reduce_scatter(lhs, w_blocks, contract, n):
    me = lax.axis_index("gx")
    half = lhs.shape[0] // 2
    top = lhs[:half]
    bottom = lhs[half:]

    def block(index):
        return lax.dynamic_index_in_dim(w_blocks, index % n, 0, keepdims=False)

    acc_top = contract(top, block(me - 1))
    acc_bottom = contract(bottom, block(me + 1))
    for step in range(1, n):
        got_top = lax.ppermute(acc_top.astype(jnp.bfloat16), "gx", ring_perm(n, 1))
        got_bottom = lax.ppermute(acc_bottom.astype(jnp.bfloat16), "gx", ring_perm(n, -1))
        acc_top = got_top.astype(jnp.float32) + contract(top, block(me - step - 1))
        acc_bottom = got_bottom.astype(jnp.float32) + contract(bottom, block(me + step + 1))
    return jnp.concatenate([acc_top, acc_bottom], axis=0)


def plain_dot(lhs, rhs):
    return jnp.dot(lhs, rhs, preferred_element_type=jnp.float32)


def merge_dot(lhs, rhs):
    return jnp.einsum("pkf,kfc->pc", lhs, rhs, preferred_element_type=jnp.float32)


def gx_sum_rows(sums, n):
    me = lax.axis_index("gx")
    relative = [sums] + [lax.ppermute(sums, "gx", ring_perm(n, -shift)) for shift in range(1, n)]
    doubled = jnp.stack(relative + relative, axis=1)
    blocks = lax.dynamic_slice_in_dim(doubled, (n - me) % n, n, axis=1)
    total = blocks[:, 0]
    for j in range(1, n):
        total = total + blocks[:, j]
    return total


def local_attention(qkv, segment_ids):
    tok_rows = qkv.shape[1]
    head_count = qkv.shape[2] // HEAD
    queries = qkv[0].reshape(tok_rows, head_count, HEAD)
    key_rows = qkv[1].reshape(tok_rows, head_count, HEAD)
    value_rows = qkv[2].reshape(tok_rows, head_count, HEAD)
    query_block = tok_rows

    def one_block(index):
        first_query = index * query_block
        query_part = lax.dynamic_slice_in_dim(queries, first_query, query_block, 0)
        query_ids = lax.dynamic_slice_in_dim(segment_ids, first_query, query_block, 0)
        scores = jnp.einsum(
            "qhe,khe->hqk", query_part, key_rows, preferred_element_type=jnp.float32
        ) * HEAD ** (-0.5)
        same_segment = query_ids[None, :, None] == segment_ids[None, None, :]
        scores = jnp.where(same_segment, scores, -1e30)
        highest = jnp.max(scores, axis=-1, keepdims=True)
        raised = jnp.exp(scores - highest)
        shares = (raised / jnp.sum(raised, axis=-1, keepdims=True)).astype(jnp.bfloat16)
        return jnp.einsum(
            "hqk,khe->qhe", shares, value_rows, preferred_element_type=jnp.float32
        ).astype(jnp.bfloat16)

    blocks = lax.map(one_block, jnp.arange(tok_rows // query_block, dtype=jnp.int32))
    return blocks.reshape(tok_rows, head_count * HEAD)


def body(
    tokens,
    segment_ids,
    first_gain,
    first_bias,
    query_key_value,
    project_out,
    second_gain,
    second_bias,
    up_weight,
    down_weight,
    final_gain,
    final_bias,
    merge_weight,
    owners,
):
    tok_rows = tokens.shape[0]
    feature_cols = tokens.shape[1]
    n_gx = lax.axis_size("gx")
    features = feature_cols * n_gx
    qkv_all = lax.all_gather(query_key_value, "gy", axis=1, tiled=True)
    proj_all = lax.all_gather(project_out, "gy", axis=1, tiled=True)
    up_all = lax.all_gather(up_weight, "gy", axis=0, tiled=True)
    down_all = lax.all_gather(down_weight, "gy", axis=1, tiled=True)
    merge_all = lax.all_gather(merge_weight, "gy", axis=2, tiled=True)
    width = feature_cols
    proj_blocks = proj_all.reshape(proj_all.shape[0], n_gx, width).transpose(1, 0, 2)
    down_blocks = down_all.reshape(down_all.shape[0], n_gx, width).transpose(1, 0, 2)
    full_rows = gx_all_gather(tokens, n_gx)
    normed = normalize_rows(full_rows, first_gain, first_bias).astype(jnp.bfloat16)
    columns = normed
    qkv = jnp.einsum(
        "td,kdc->ktc",
        columns,
        qkv_all,
        preferred_element_type=jnp.float32,
    ).astype(jnp.bfloat16)
    attended = local_attention(qkv, segment_ids)
    attn_share = gx_matmul_reduce_scatter(attended, proj_blocks, plain_dot, n_gx)
    first_resid = (tokens.astype(jnp.float32) + attn_share).astype(jnp.bfloat16)
    resid_rows = gx_all_gather(first_resid, n_gx)
    second_normed = normalize_rows(resid_rows, second_gain, second_bias).astype(jnp.bfloat16)
    columns = second_normed
    upper = jnp.dot(
        columns,
        up_all,
        preferred_element_type=jnp.float32,
    )
    hidden = jax.nn.gelu(upper, approximate=False).astype(jnp.bfloat16)
    mlp_share = gx_matmul_reduce_scatter(hidden, down_blocks, plain_dot, n_gx)
    second_resid = (first_resid.astype(jnp.float32) + mlp_share).astype(jnp.bfloat16)
    post_sums = gx_sum_rows(jnp.stack(row_sums(second_resid)), n_gx)
    final_normed = normalize_from_sums(
        second_resid,
        post_sums,
        features,
        own_slice(final_gain, feature_cols),
        own_slice(final_bias, feature_cols),
    ).astype(jnp.bfloat16)
    merged_rows = tok_rows // 4
    grouped = (
        final_normed.reshape(tok_rows // (2 * IMG_W), 2, IMG_W // 2, 2, feature_cols)
        .transpose(0, 2, 1, 3, 4)
        .reshape(merged_rows, 4, feature_cols)
    )
    merge_terms = merge_dot(grouped, merge_all)
    projected = gx_reduce_scatter(merge_terms, n_gx).astype(jnp.bfloat16)
    owner_count = lax.axis_size("gy")
    capacity = max(2, 2 * merged_rows // owner_count)
    owner_col = owners[:, 0]
    one_hot = (owner_col[:, None] == jnp.arange(owner_count, dtype=jnp.int32)[None, :]).astype(
        jnp.int32
    )
    slot_rank = jnp.sum((jnp.cumsum(one_hot, axis=0) - 1) * one_hot, axis=1)
    target = jnp.where(slot_rank < capacity, owner_col * capacity + slot_rank, -1)
    picks = (
        target[None, :] == jnp.arange(owner_count * capacity, dtype=jnp.int32)[:, None]
    ).astype(jnp.bfloat16)
    outgoing = jnp.dot(picks, projected, preferred_element_type=jnp.float32).astype(
        jnp.bfloat16
    ).reshape(owner_count, capacity, feature_cols)
    arrived = lax.all_to_all(outgoing, "gy", split_axis=0, concat_axis=0, tiled=True)
    return arrived.reshape(1, owner_count, capacity, feature_cols)


def solution(mesh):
    in_specs = (
        P("gy", "gx"),
        P("gy"),
        P(),
        P(),
        P(None, "gy", "gx"),
        P("gx", "gy"),
        P(),
        P(),
        P("gy", "gx"),
        P("gx", "gy"),
        P(),
        P(),
        P(None, "gx", "gy"),
        P("gy", None),
    )
    out_specs = P("gy", None, None, "gx")

    return jax.shard_map(body, mesh=mesh, in_specs=in_specs, out_specs=out_specs, check_vma=False)
```

```python
import jax
import jax.numpy as jnp
from jax import lax
from jax.sharding import PartitionSpec as P

HEAD = 104
IMG_W = 16


EPSILON = 1e-06


def normalize_rows(values, gain, bias):
    values = values.astype(jnp.float32)
    center = values - jnp.mean(values, axis=-1, keepdims=True)
    spread = jnp.mean(center * center, axis=-1, keepdims=True)
    return center * lax.rsqrt(spread + EPSILON) * gain + bias


def normalize_from_sums(values, sums, features, gain, bias):
    values = values.astype(jnp.float32)
    row_mean = sums[0] / features
    spread = sums[1] / features - row_mean * row_mean
    return (values - row_mean[:, None]) * lax.rsqrt(spread[:, None] + EPSILON) * gain + bias


def own_slice(vector, width):
    return lax.dynamic_slice_in_dim(vector, lax.axis_index("gx") * width, width, 0)


def row_sums(values):
    values = values.astype(jnp.float32)
    return (jnp.sum(values, axis=-1), jnp.sum(values * values, axis=-1))


def ring_perm(n, shift):
    return [(j, (j + shift) % n) for j in range(n)]


def gx_all_gather(x, n):
    me = lax.axis_index("gx")
    half = x.shape[0] // 2
    from_left = lax.ppermute(x, "gx", ring_perm(n, 1))
    from_right = lax.ppermute(x, "gx", ring_perm(n, -1))
    far_top = lax.ppermute(from_left[:half], "gx", ring_perm(n, 1))
    far_bottom = lax.ppermute(from_right[half:], "gx", ring_perm(n, -1))
    far = jnp.concatenate([far_top, far_bottom], axis=0)
    relative = [x, from_right, far, from_left]
    columns = []
    for j in range(n):
        offset = (j - me) % n
        block = relative[n - 1]
        for k in range(n - 2, -1, -1):
            block = jnp.where(offset == k, relative[k], block)
        columns.append(block)
    return jnp.concatenate(columns, axis=1)


def gx_reduce_scatter(y, n):
    me = lax.axis_index("gx")
    rows = y.shape[0]
    width = y.shape[1] // n
    half = rows // 2
    blocks = y.reshape(rows, n, width)

    def own(part, index):
        return lax.dynamic_slice_in_dim(part, index % n, 1, axis=1)[:, 0]

    top = blocks[:half]
    bottom = blocks[half:]
    acc_top = own(top, me - 1)
    acc_bottom = own(bottom, me + 1)
    for step in range(1, n):
        got_top = lax.ppermute(acc_top.astype(jnp.bfloat16), "gx", ring_perm(n, 1))
        got_bottom = lax.ppermute(acc_bottom.astype(jnp.bfloat16), "gx", ring_perm(n, -1))
        acc_top = got_top.astype(jnp.float32) + own(top, me - step - 1)
        acc_bottom = got_bottom.astype(jnp.float32) + own(bottom, me + step + 1)
    return jnp.concatenate([acc_top, acc_bottom], axis=0)


def gx_matmul_reduce_scatter(lhs, w_blocks, contract, n):
    me = lax.axis_index("gx")
    half = lhs.shape[0] // 2
    top = lhs[:half]
    bottom = lhs[half:]

    def block(index):
        return lax.dynamic_index_in_dim(w_blocks, index % n, 0, keepdims=False)

    acc_top = contract(top, block(me - 1))
    acc_bottom = contract(bottom, block(me + 1))
    for step in range(1, n):
        got_top = lax.ppermute(acc_top.astype(jnp.bfloat16), "gx", ring_perm(n, 1))
        got_bottom = lax.ppermute(acc_bottom.astype(jnp.bfloat16), "gx", ring_perm(n, -1))
        acc_top = got_top.astype(jnp.float32) + contract(top, block(me - step - 1))
        acc_bottom = got_bottom.astype(jnp.float32) + contract(bottom, block(me + step + 1))
    return jnp.concatenate([acc_top, acc_bottom], axis=0)


def plain_dot(lhs, rhs):
    return jnp.dot(lhs, rhs, preferred_element_type=jnp.float32)


def merge_dot(lhs, rhs):
    return jnp.einsum("pkf,kfc->pc", lhs, rhs, preferred_element_type=jnp.float32)


def gx_sum_rows(sums, n):
    me = lax.axis_index("gx")
    relative = [sums] + [lax.ppermute(sums, "gx", ring_perm(n, -shift)) for shift in range(1, n)]
    doubled = jnp.stack(relative + relative, axis=1)
    blocks = lax.dynamic_slice_in_dim(doubled, (n - me) % n, n, axis=1)
    total = blocks[:, 0]
    for j in range(1, n):
        total = total + blocks[:, j]
    return total


def local_attention(qkv, segment_ids):
    tok_rows = qkv.shape[1]
    head_count = qkv.shape[2] // HEAD
    queries = qkv[0].reshape(tok_rows, head_count, HEAD)
    key_rows = qkv[1].reshape(tok_rows, head_count, HEAD)
    value_rows = qkv[2].reshape(tok_rows, head_count, HEAD)
    query_block = tok_rows

    def one_block(index):
        first_query = index * query_block
        query_part = lax.dynamic_slice_in_dim(queries, first_query, query_block, 0)
        query_ids = lax.dynamic_slice_in_dim(segment_ids, first_query, query_block, 0)
        scores = jnp.einsum(
            "qhe,khe->hqk", query_part, key_rows, preferred_element_type=jnp.float32
        ) * HEAD ** (-0.5)
        same_segment = query_ids[None, :, None] == segment_ids[None, None, :]
        scores = jnp.where(same_segment, scores, -1e30)
        highest = jnp.max(scores, axis=-1, keepdims=True)
        raised = jnp.exp(scores - highest)
        shares = (raised / jnp.sum(raised, axis=-1, keepdims=True)).astype(jnp.bfloat16)
        return jnp.einsum(
            "hqk,khe->qhe", shares, value_rows, preferred_element_type=jnp.float32
        ).astype(jnp.bfloat16)

    blocks = lax.map(one_block, jnp.arange(tok_rows // query_block, dtype=jnp.int32))
    return blocks.reshape(tok_rows, head_count * HEAD)


def body(
    tokens,
    segment_ids,
    first_gain,
    first_bias,
    query_key_value,
    project_out,
    second_gain,
    second_bias,
    up_weight,
    down_weight,
    final_gain,
    final_bias,
    merge_weight,
    owners,
):
    tok_rows = tokens.shape[0]
    feature_cols = tokens.shape[1]
    n_gx = lax.axis_size("gx")
    features = feature_cols * n_gx
    planes = jnp.concatenate([query_key_value, project_out.T[None]], axis=0)
    planes_all = lax.all_gather(planes, "gy", axis=1, tiled=True)
    qkv_all = planes_all[: query_key_value.shape[0]]
    proj_all = planes_all[query_key_value.shape[0]].T
    up_all = lax.all_gather(up_weight, "gy", axis=0, tiled=True)
    down_all = lax.all_gather(down_weight, "gy", axis=1, tiled=True)
    merge_all = lax.all_gather(merge_weight, "gy", axis=2, tiled=True)
    width = feature_cols
    proj_blocks = proj_all.reshape(proj_all.shape[0], n_gx, width).transpose(1, 0, 2)
    down_blocks = down_all.reshape(down_all.shape[0], n_gx, width).transpose(1, 0, 2)
    full_rows = gx_all_gather(tokens, n_gx)
    normed = normalize_rows(full_rows, first_gain, first_bias).astype(jnp.bfloat16)
    columns = normed
    qkv = jnp.einsum(
        "td,kdc->ktc",
        columns,
        qkv_all,
        preferred_element_type=jnp.float32,
    ).astype(jnp.bfloat16)
    attended = local_attention(qkv, segment_ids)
    attn_share = gx_matmul_reduce_scatter(attended, proj_blocks, plain_dot, n_gx)
    first_resid = (tokens.astype(jnp.float32) + attn_share).astype(jnp.bfloat16)
    resid_rows = gx_all_gather(first_resid, n_gx)
    second_normed = normalize_rows(resid_rows, second_gain, second_bias).astype(jnp.bfloat16)
    columns = second_normed
    upper = jnp.dot(
        columns,
        up_all,
        preferred_element_type=jnp.float32,
    )
    hidden = jax.nn.gelu(upper, approximate=False).astype(jnp.bfloat16)
    mlp_share = gx_matmul_reduce_scatter(hidden, down_blocks, plain_dot, n_gx)
    second_resid = (first_resid.astype(jnp.float32) + mlp_share).astype(jnp.bfloat16)
    post_sums = gx_sum_rows(jnp.stack(row_sums(second_resid)), n_gx)
    final_normed = normalize_from_sums(
        second_resid,
        post_sums,
        features,
        own_slice(final_gain, feature_cols),
        own_slice(final_bias, feature_cols),
    ).astype(jnp.bfloat16)
    merged_rows = tok_rows // 4
    grouped = (
        final_normed.reshape(tok_rows // (2 * IMG_W), 2, IMG_W // 2, 2, feature_cols)
        .transpose(0, 2, 1, 3, 4)
        .reshape(merged_rows, 4, feature_cols)
    )
    merge_terms = merge_dot(grouped, merge_all)
    projected = gx_reduce_scatter(merge_terms, n_gx).astype(jnp.bfloat16)
    owner_count = lax.axis_size("gy")
    capacity = max(2, 2 * merged_rows // owner_count)
    owner_col = owners[:, 0]
    one_hot = (owner_col[:, None] == jnp.arange(owner_count, dtype=jnp.int32)[None, :]).astype(
        jnp.int32
    )
    slot_rank = jnp.sum((jnp.cumsum(one_hot, axis=0) - 1) * one_hot, axis=1)
    target = jnp.where(slot_rank < capacity, owner_col * capacity + slot_rank, -1)
    picks = (
        target[None, :] == jnp.arange(owner_count * capacity, dtype=jnp.int32)[:, None]
    ).astype(jnp.bfloat16)
    outgoing = jnp.dot(picks, projected, preferred_element_type=jnp.float32).astype(
        jnp.bfloat16
    ).reshape(owner_count, capacity, feature_cols)
    arrived = lax.all_to_all(outgoing, "gy", split_axis=0, concat_axis=0, tiled=True)
    return arrived.reshape(1, owner_count, capacity, feature_cols)


def solution(mesh):
    in_specs = (
        P("gy", "gx"),
        P("gy"),
        P(),
        P(),
        P(None, "gy", "gx"),
        P("gx", "gy"),
        P(),
        P(),
        P("gy", "gx"),
        P("gx", "gy"),
        P(),
        P(),
        P(None, "gx", "gy"),
        P("gy", None),
    )
    out_specs = P("gy", None, None, "gx")

    return jax.shard_map(body, mesh=mesh, in_specs=in_specs, out_specs=out_specs, check_vma=False)
```
